512 devices in a mesh: seq: 128 (over y, x, z_hi, core), ch: 4 (over z_lo).
Axes of the slice: x: 4, y: 4, z: 16 (z_hi: 4, z_lo: 4; z = z_hi * 4 + z_lo), core: 2. Of those that a mesh axis runs over, the one named last changes fastest.
Arguments:
- signal: bfloat16 [256, 32768], P('ch', 'seq'), may hold values from -400 to 400
- long_filter: float32 [256, 32768], P('ch', 'seq'), may hold values from -1.8 to 1.8
- skip_weight: float32 [256], P('ch'), may hold values from 0.5 to 1.5
- short_taps: float32 [7, 256], P(None, 'ch'), may hold values from -2 to 2
- norm_gain: float32 [256], P('ch'), may hold values from 0.5 to 1.5
Outputs:
- normed: float32 [256, 32768], P('ch', 'seq')
The draws below stay inside these ranges and needn't reach their ends.
All inputs are finite; a program needn't handle non-finite values.
Results may differ from the reference program's by a relative error of at most 0.0003.
Values sent between devices are 32-bit elements; how exact they have to be, the bound alone decides.
No kernel may reach another device: no remote copies, remote signals or barrier semaphores. Data moves between devices by JAX's collectives and lax.ppermute only.
A program may use at most 64 MiB of HBM per device.

```python
import math
import jax
import jax.numpy as jnp
from jax import lax

CHANNELS = 256
TAPS = 7
CONTEXT_SPAN = 32768


def draw_signal(key, part):
    key_jitter_random, key_token, key_channel = jax.random.split(key, 3)
    samples = jnp.clip(jax.random.normal(key_jitter_random, (CHANNELS, CONTEXT_SPAN), jnp.float32), -4.0, 4.0)
    token_scale = 10.0 ** jax.random.uniform(key_token, (1, CONTEXT_SPAN), jnp.float32)
    position = jnp.arange(CHANNELS, dtype=jnp.float32) / CHANNELS
    channel_scale = 10.0 ** (0.5 * position + 0.5 * jax.random.uniform(key_channel, (CHANNELS,), jnp.float32))
    return (samples * token_scale * channel_scale[:, None]).astype(jnp.bfloat16)


def draw_long_filter(key, part):
    key_jitter_random, key_select_random, key_gradual_random, key_quick_random, peak_draw_seed, key_retain_random = jax.random.split(key, 6)
    length_f = float(CONTEXT_SPAN)
    slow_share = 0.5
    samples = jnp.clip(jax.random.normal(key_jitter_random, (CHANNELS, CONTEXT_SPAN), jnp.float32), -4.0, 4.0)
    is_slow = jax.random.uniform(key_select_random, (CHANNELS,), jnp.float32) < slow_share
    slow_rate = jnp.exp(jax.random.uniform(key_gradual_random, (CHANNELS,), jnp.float32, math.log(0.1 / length_f), math.log(2.0 / length_f)))
    fast_rate = jnp.exp(jax.random.uniform(key_quick_random, (CHANNELS,), jnp.float32, math.log(2.0 / length_f), math.log(1.0 / 30.0)))
    decay_rate = jnp.where(is_slow, slow_rate, fast_rate)
    lagged_offsets = jnp.arange(CONTEXT_SPAN, dtype=jnp.float32)[None, :]
    falloff_profile = jnp.exp(-decay_rate[:, None] * lagged_offsets)
    cluster_onset = jax.random.randint(peak_draw_seed, (4,), 1, CONTEXT_SPAN).astype(jnp.float32)
    surviving_proportion = jax.random.uniform(key_retain_random, (4, CHANNELS), jnp.float32, 0.5, 0.8)
    for peak_slot in range(4):
        falloff_profile = falloff_profile * jnp.where(lagged_offsets >= cluster_onset[peak_slot], surviving_proportion[peak_slot][:, None], 1.0)
    amplitude = jnp.sqrt(2.0 * decay_rate + 1.0 / length_f)
    return (samples * falloff_profile * amplitude[:, None]).astype(jnp.float32)


def level_of(stream_key, shape, shards, low, high):
    level = 1.0
    for axis_at, blocks in shards:
        steps = jax.random.uniform(jax.random.fold_in(jax.random.fold_in(stream_key, 6), axis_at), (blocks,), jnp.float32, low / len(shards), high / len(shards))
        level = level * jnp.repeat(jnp.exp(steps), shape[axis_at] // blocks).reshape((-1,) + (1,) * (len(shape) - 1 - axis_at))
    return level


def gaussian(stream_key, shape, spread, limit, shards=(), kind=jnp.bfloat16):
    values = spread * jax.random.normal(stream_key, shape, jnp.float32)
    if shards:
        values = values * level_of(stream_key, shape, shards, -0.22, 0.18)
    return jnp.clip(values, -limit, limit).astype(kind)


def setup_inputs(seed: int = 0) -> dict:
    streams_of = jax.random.split(jax.random.key(seed), 6)
    return {
        "signal": draw_signal(jax.random.fold_in(streams_of[5], 71), 0),
        "long_filter": draw_long_filter(jax.random.fold_in(streams_of[5], 71), 0),
        "skip_weight": jnp.clip(0.5 + 1.0 * jax.random.uniform(streams_of[2], (CHANNELS,), jnp.float32) ** level_of(streams_of[2], (CHANNELS,), ((0, 4),), -0.2, 0.2), 0.5, 1.5),
        "short_taps": gaussian(streams_of[3], (TAPS, CHANNELS), TAPS ** -0.5, 2.0, ((1, 4),), jnp.float32),
        "norm_gain": jnp.clip(1.0 + 0.1 * jax.random.normal(streams_of[4], (CHANNELS,), jnp.float32), 0.5, 1.5),
    }


def causal_block(pair_args):
    signal_block, filter_block = pair_args
    doubled = 2 * CONTEXT_SPAN
    spectrum = jnp.fft.rfft(signal_block, n=doubled, axis=1) * jnp.fft.rfft(filter_block, n=doubled, axis=1)
    return jnp.fft.irfft(spectrum, n=doubled, axis=1)[:, :CONTEXT_SPAN].astype(signal_block.dtype)

def reference(signal, long_filter, skip_weight, short_taps, norm_gain):
    signal_f = signal.astype(jnp.float32)
    block_width = min(CHANNELS, 32)
    groups = CHANNELS // block_width
    stacked = (signal_f.reshape(groups, block_width, CONTEXT_SPAN), long_filter.reshape(groups, block_width, CONTEXT_SPAN))
    conv = lax.map(causal_block, stacked).reshape(CHANNELS, CONTEXT_SPAN)
    mixed_rows = conv + skip_weight[:, None] * signal_f
    padded = jnp.concatenate([jnp.zeros((CHANNELS, TAPS - 1), mixed_rows.dtype), mixed_rows], 1)
    short_conv = jnp.zeros_like(mixed_rows)
    for offset in range(TAPS):
        start_row = TAPS - 1 - offset
        short_conv = short_conv + short_taps[offset][:, None] * padded[:, start_row:start_row + CONTEXT_SPAN]
    energy = lax.optimization_barrier(jnp.mean(short_conv * short_conv, axis=0, keepdims=True))
    return short_conv * norm_gain[:, None] * lax.rsqrt(energy + 1e-06)
```

```python
import math

import jax
import jax.numpy as jnp
from jax import lax
from jax.sharding import PartitionSpec as P

highest = lax.Precision.HIGHEST


def phases(left_ids, right_ids, modulus, direction):
    product = left_ids[:, None] * right_ids[None, :] % modulus
    angles = product.astype(jnp.float32) * (2.0 * math.pi / modulus)
    return (jnp.cos(angles), direction * jnp.sin(angles))


def mat(a, b):
    return jnp.dot(a, b, precision=highest, preferred_element_type=jnp.float32)


def cmat(ar, ai, br, bi):
    if ai is None:
        return (mat(ar, br), mat(ar, bi))
    if bi is None:
        return (mat(ar, br), mat(ai, br))
    return (mat(ar, br) - mat(ai, bi), mat(ar, bi) + mat(ai, br))


def cmul(ar, ai, br, bi):
    return (ar * br - ai * bi, ar * bi + ai * br)


def local(signal, long_filter, skip_weight, short_taps, norm_gain):
    seq_parts = lax.axis_size("seq")
    width, length = signal.shape
    dup = seq_parts // width
    piece = length // dup
    own = lax.axis_index("seq")
    chan = own // dup
    half = own % dup
    signal_f = signal.astype(jnp.float32)

    both = jnp.stack([signal_f, long_filter], 1)
    send = jnp.repeat(both, dup, axis=0)
    recv = lax.all_to_all(send, "seq", 0, 0, tiled=True)
    x_rows = recv[:, 0, :]
    h_rows = recv[:, 1, :]

    rows = 2 * seq_parts
    cols = length
    modulus = rows * cols
    row_ids = jnp.arange(rows, dtype=jnp.int32)
    live_ids = jnp.arange(seq_parts, dtype=jnp.int32)
    col_ids = jnp.arange(cols, dtype=jnp.int32)
    rows_fwd = phases(row_ids, live_ids, rows, -1.0)
    turn_fwd = phases(row_ids, col_ids, modulus, -1.0)
    cols_fwd = phases(col_ids, col_ids, cols, -1.0)
    cols_inv = phases(col_ids, col_ids, cols, 1.0)
    rows_inv = phases(live_ids, row_ids, rows, 1.0)

    def forward(x):
        yr, yi = cmat(rows_fwd[0], rows_fwd[1], x, None)
        yr, yi = cmul(yr, yi, turn_fwd[0], turn_fwd[1])
        return cmat(yr, yi, cols_fwd[0], cols_fwd[1])

    xr, xi = forward(x_rows)
    hr, hi = forward(h_rows)
    pr, pi = cmul(xr, xi, hr, hi)
    qr, qi = cmat(pr, pi, cols_inv[0], cols_inv[1])
    qr, qi = cmul(qr, qi, turn_fwd[0], -turn_fwd[1])
    conv = (mat(rows_inv[0], qr) - mat(rows_inv[1], qi)) * (1.0 / modulus)

    skip = lax.dynamic_index_in_dim(skip_weight, chan, keepdims=False)
    mixed = (conv + skip * x_rows).reshape(seq_parts * length)
    tap_count = short_taps.shape[0]
    taps = lax.dynamic_index_in_dim(short_taps, chan, axis=1, keepdims=False)
    padded = jnp.concatenate([jnp.zeros((tap_count - 1,), mixed.dtype), mixed])
    total = seq_parts * length
    short = jnp.zeros_like(mixed)
    for offset in range(tap_count):
        start = tap_count - 1 - offset
        short = short + taps[offset] * padded[start : start + total]
    short_rows = short.reshape(seq_parts, length)
    back = lax.dynamic_slice_in_dim(short_rows, half * piece, piece, axis=1)
    got = lax.all_to_all(back, "seq", 0, 0, tiled=True)
    short_local = got.reshape(width, length)

    energy = lax.psum(jnp.sum(short_local * short_local, 0), "ch")
    all_channels = width * lax.axis_size("ch")
    return short_local * norm_gain[:, None] * lax.rsqrt(energy / all_channels + 1e-06)[None, :]


def solution(mesh):
    return jax.shard_map(
        local,
        mesh=mesh,
        in_specs=(P("ch", "seq"), P("ch", "seq"), P("ch"), P(None, "ch"), P("ch")),
        out_specs=P("ch", "seq"),
        check_vma=False,
    )
```

```python
import math

import jax
import jax.numpy as jnp
from jax import lax
from jax.sharding import PartitionSpec as P

highest = lax.Precision.HIGH


def phases(left_ids, right_ids, modulus, direction):
    product = left_ids[:, None] * right_ids[None, :] % modulus
    angles = product.astype(jnp.float32) * (2.0 * math.pi / modulus)
    return (jnp.cos(angles), direction * jnp.sin(angles))


def mat(a, b):
    return jnp.dot(a, b, precision=highest, preferred_element_type=jnp.float32)


def cmat(ar, ai, br, bi):
    if ai is None:
        return (mat(ar, br), mat(ar, bi))
    if bi is None:
        return (mat(ar, br), mat(ai, br))
    return (mat(ar, br) - mat(ai, bi), mat(ar, bi) + mat(ai, br))


def cmul(ar, ai, br, bi):
    return (ar * br - ai * bi, ar * bi + ai * br)


def local(signal, long_filter, skip_weight, short_taps, norm_gain):
    seq_parts = lax.axis_size("seq")
    width, length = signal.shape
    dup = seq_parts // width
    piece = length // dup
    own = lax.axis_index("seq")
    chan = own // dup
    half = own % dup
    signal_f = signal.astype(jnp.float32)

    both = jnp.stack([signal_f, long_filter], 1)
    send = jnp.repeat(both, dup, axis=0)
    recv = lax.all_to_all(send, "seq", 0, 0, tiled=True)
    x_rows = recv[:, 0, :]
    h_rows = recv[:, 1, :]

    rows = 2 * seq_parts
    cols = length
    modulus = rows * cols
    row_ids = jnp.arange(rows, dtype=jnp.int32)
    col_ids = jnp.arange(cols, dtype=jnp.int32)
    square = phases(col_ids, col_ids, cols, 1.0)
    turn = phases(row_ids, col_ids, modulus, 1.0)
    square, turn = lax.optimization_barrier((square, turn))
    rows_fwd = (square[0][:, :seq_parts], -square[1][:, :seq_parts])
    turn_fwd = (turn[0], -turn[1])
    cols_fwd = (square[0], -square[1])
    cols_inv = square
    rows_inv = (square[0][:seq_parts], square[1][:seq_parts])

    def forward(x):
        yr, yi = cmat(rows_fwd[0], rows_fwd[1], x, None)
        yr, yi = cmul(yr, yi, turn_fwd[0], turn_fwd[1])
        return cmat(yr, yi, cols_fwd[0], cols_fwd[1])

    xr, xi = forward(x_rows)
    hr, hi = forward(h_rows)
    pr, pi = cmul(xr, xi, hr, hi)
    qr, qi = cmat(pr, pi, cols_inv[0], cols_inv[1])
    qr, qi = cmul(qr, qi, turn_fwd[0], -turn_fwd[1])
    conv = (mat(rows_inv[0], qr) - mat(rows_inv[1], qi)) * (1.0 / modulus)

    skip = lax.dynamic_index_in_dim(skip_weight, chan, keepdims=False)
    mixed = (conv + skip * x_rows).reshape(seq_parts * length)
    tap_count = short_taps.shape[0]
    taps = lax.dynamic_index_in_dim(short_taps, chan, axis=1, keepdims=False)
    padded = jnp.concatenate([jnp.zeros((tap_count - 1,), mixed.dtype), mixed])
    total = seq_parts * length
    short = jnp.zeros_like(mixed)
    for offset in range(tap_count):
        start = tap_count - 1 - offset
        short = short + taps[offset] * padded[start : start + total]
    short_rows = short.reshape(seq_parts, length)
    back = lax.dynamic_slice_in_dim(short_rows, half * piece, piece, axis=1)
    got = lax.all_to_all(back, "seq", 0, 0, tiled=True)
    short_local = got.reshape(width, length)

    energy = lax.psum(jnp.sum(short_local * short_local, 0), "ch")
    all_channels = width * lax.axis_size("ch")
    return short_local * norm_gain[:, None] * lax.rsqrt(energy / all_channels + 1e-06)[None, :]


def solution(mesh):
    return jax.shard_map(
        local,
        mesh=mesh,
        in_specs=(P("ch", "seq"), P("ch", "seq"), P("ch"), P(None, "ch"), P("ch")),
        out_specs=P("ch", "seq"),
        check_vma=False,
    )
```

```python
import math

import jax
import jax.numpy as jnp
from jax import lax
from jax.sharding import PartitionSpec as P

highest = lax.Precision.HIGH


def phases(left_ids, right_ids, modulus, direction):
    product = left_ids[:, None] * right_ids[None, :] % modulus
    angles = product.astype(jnp.float32) * (2.0 * math.pi / modulus)
    return (jnp.cos(angles), direction * jnp.sin(angles))


def mat(a, b):
    return jnp.dot(a, b, precision=highest, preferred_element_type=jnp.float32)


def cmat(ar, ai, br, bi):
    if ai is None:
        return (mat(ar, br), mat(ar, bi))
    if bi is None:
        return (mat(ar, br), mat(ai, br))
    return (mat(ar, br) - mat(ai, bi), mat(ar, bi) + mat(ai, br))


def cmul(ar, ai, br, bi):
    return (ar * br - ai * bi, ar * bi + ai * br)


def local(signal, long_filter, skip_weight, short_taps, norm_gain):
    seq_parts = lax.axis_size("seq")
    width, length = signal.shape
    dup = seq_parts // width
    piece = length // dup
    own = lax.axis_index("seq")
    chan = own // dup
    half = own % dup
    signal_f = signal.astype(jnp.float32)

    both = jnp.stack([signal_f, long_filter], 1)
    send = jnp.repeat(both, dup, axis=0)
    recv = lax.all_to_all(send, "seq", 0, 0, tiled=True)
    x_rows = recv[:, 0, :]
    h_rows = recv[:, 1, :]

    rows = 2 * seq_parts
    cols = length
    modulus = rows * cols
    row_ids = jnp.arange(rows, dtype=jnp.int32)
    col_ids = jnp.arange(cols, dtype=jnp.int32)
    square = phases(col_ids, col_ids, cols, 1.0)
    turn = phases(row_ids, col_ids, modulus, 1.0)
    square, turn = lax.optimization_barrier((square, turn))
    rows_fwd = (square[0][:, :seq_parts], -square[1][:, :seq_parts])
    turn_fwd = (turn[0], -turn[1])
    cols_fwd = (square[0], -square[1])
    cols_inv = square
    rows_inv = (square[0][:seq_parts], square[1][:seq_parts])

    def forward(x):
        yr, yi = cmat(rows_fwd[0], rows_fwd[1], x, None)
        yr, yi = cmul(yr, yi, turn_fwd[0], turn_fwd[1])
        return cmat(yr, yi, cols_fwd[0], cols_fwd[1])

    xr, xi = forward(x_rows)
    hr, hi = forward(h_rows)
    pr, pi = cmul(xr, xi, hr, hi)
    qr, qi = cmat(pr, pi, cols_inv[0], cols_inv[1])
    qr, qi = cmul(qr, qi, turn_fwd[0], -turn_fwd[1])
    conv = (mat(rows_inv[0], qr) - mat(rows_inv[1], qi)) * (1.0 / modulus)

    skip = lax.dynamic_index_in_dim(skip_weight, chan, keepdims=False)
    mixed = (conv + skip * x_rows).reshape(seq_parts * length)
    tap_count = short_taps.shape[0]
    taps = lax.dynamic_index_in_dim(short_taps, chan, axis=1, keepdims=False)
    padded = jnp.concatenate([jnp.zeros((tap_count - 1,), mixed.dtype), mixed])
    total = seq_parts * length
    short = jnp.zeros_like(mixed)
    for offset in range(tap_count):
        start = tap_count - 1 - offset
        short = short + taps[offset] * padded[start : start + total]
    short_rows = short.reshape(seq_parts, length)
    back = lax.dynamic_slice_in_dim(short_rows, half * piece, piece, axis=1)
    groups = lax.axis_size("ch")
    spread = jnp.tile(back, (groups, 1))
    got = lax.all_to_all(spread, ("ch", "seq"), 0, 0, tiled=True)
    every = got.reshape(groups, width, length)
    energy = jnp.sum(every * every, (0, 1))
    short_local = lax.dynamic_index_in_dim(every, lax.axis_index("ch"), keepdims=False)
    all_channels = width * groups
    return short_local * norm_gain[:, None] * lax.rsqrt(energy / all_channels + 1e-06)[None, :]


def solution(mesh):
    return jax.shard_map(
        local,
        mesh=mesh,
        in_specs=(P("ch", "seq"), P("ch", "seq"), P("ch"), P(None, "ch"), P("ch")),
        out_specs=P("ch", "seq"),
        check_vma=False,
    )
```

```python
import math

import jax
import jax.numpy as jnp
from jax import lax
from jax.sharding import PartitionSpec as P

highest = lax.Precision.HIGH


def phases(left_ids, right_ids, modulus, direction):
    product = left_ids[:, None] * right_ids[None, :] % modulus
    angles = product.astype(jnp.float32) * (2.0 * math.pi / modulus)
    return (jnp.cos(angles), direction * jnp.sin(angles))


def mat(a, b):
    return jnp.dot(a, b, precision=highest, preferred_element_type=jnp.float32)


def cmat(ar, ai, br, bi):
    if ai is None:
        return (mat(ar, br), mat(ar, bi))
    if bi is None:
        return (mat(ar, br), mat(ai, br))
    return (mat(ar, br) - mat(ai, bi), mat(ar, bi) + mat(ai, br))


def cmul(ar, ai, br, bi):
    return (ar * br - ai * bi, ar * bi + ai * br)


def local(signal, long_filter, skip_weight, short_taps, norm_gain):
    seq_parts = lax.axis_size("seq")
    width, length = signal.shape
    dup = seq_parts // width
    piece = length // dup
    own = lax.axis_index("seq")
    chan = own // dup
    half = own % dup
    signal_f = signal.astype(jnp.float32)

    both = jnp.stack([signal_f, long_filter], 1)
    send = jnp.repeat(both, dup, axis=0)
    recv = lax.all_to_all(send, "seq", 0, 0, tiled=True)
    x_rows = recv[:, 0, :]
    h_rows = recv[:, 1, :]

    rows = 2 * seq_parts
    cols = length
    modulus = rows * cols
    row_ids = jnp.arange(rows, dtype=jnp.int32)
    col_ids = jnp.arange(cols, dtype=jnp.int32)
    square = phases(col_ids, col_ids, cols, 1.0)
    turn = phases(row_ids, col_ids, modulus, 1.0)
    square, turn = lax.optimization_barrier((square, turn))
    rows_fwd = (square[0][:, :seq_parts], -square[1][:, :seq_parts])
    turn_fwd = (turn[0], -turn[1])
    cols_fwd = (square[0], -square[1])
    cols_inv = square
    rows_inv = (square[0][:seq_parts], square[1][:seq_parts])

    def forward(x):
        yr, yi = cmat(rows_fwd[0], rows_fwd[1], x, None)
        yr, yi = cmul(yr, yi, turn_fwd[0], turn_fwd[1])
        return cmat(yr, yi, cols_fwd[0], cols_fwd[1])

    xr, xi = forward(x_rows)
    hr, hi = forward(h_rows)
    pr, pi = cmul(xr, xi, hr, hi)
    qr, qi = cmat(pr, pi, cols_inv[0], cols_inv[1])
    qr, qi = cmul(qr, qi, turn_fwd[0], -turn_fwd[1])
    conv = (mat(rows_inv[0], qr) - mat(rows_inv[1], qi)) * (1.0 / modulus)

    skip = lax.dynamic_index_in_dim(skip_weight, chan, keepdims=False)
    mixed = conv + skip * x_rows
    tap_count = short_taps.shape[0]
    taps = lax.dynamic_index_in_dim(short_taps, chan, axis=1, keepdims=False)
    rim = tap_count - 1
    tails = jnp.concatenate([jnp.zeros((1, rim), mixed.dtype), mixed[:-1, length - rim :]], 0)
    extended = jnp.concatenate([tails, mixed], 1)
    window = lax.dynamic_slice_in_dim(extended, half * piece, piece + rim, axis=1)
    back = jnp.zeros((seq_parts, piece), mixed.dtype)
    for offset in range(tap_count):
        start = rim - offset
        back = back + taps[offset] * window[:, start : start + piece]
    got = lax.all_to_all(back, "seq", 0, 0, tiled=True)
    short_local = got.reshape(width, length)

    energy = lax.psum(jnp.sum(short_local * short_local, 0), "ch")
    all_channels = width * lax.axis_size("ch")
    return short_local * norm_gain[:, None] * lax.rsqrt(energy / all_channels + 1e-06)[None, :]


def solution(mesh):
    return jax.shard_map(
        local,
        mesh=mesh,
        in_specs=(P("ch", "seq"), P("ch", "seq"), P("ch"), P(None, "ch"), P("ch")),
        out_specs=P("ch", "seq"),
        check_vma=False,
    )
```

```python
import math

import jax
import jax.numpy as jnp
from jax import lax
from jax.sharding import PartitionSpec as P

highest = lax.Precision.HIGH


def phases(left_ids, right_ids, modulus, direction):
    product = left_ids[:, None] * right_ids[None, :] % modulus
    angles = product.astype(jnp.float32) * (2.0 * math.pi / modulus)
    return (jnp.cos(angles), direction * jnp.sin(angles))


def mat(a, b):
    return jnp.dot(a, b, precision=highest, preferred_element_type=jnp.float32)


def cmat(ar, ai, br, bi):
    if ai is None:
        return (mat(ar, br), mat(ar, bi))
    if bi is None:
        return (mat(ar, br), mat(ai, br))
    return (mat(ar, br) - mat(ai, bi), mat(ar, bi) + mat(ai, br))


def cmul(ar, ai, br, bi):
    return (ar * br - ai * bi, ar * bi + ai * br)


def local(signal, long_filter, skip_weight, short_taps, norm_gain):
    seq_parts = lax.axis_size("seq")
    width, length = signal.shape
    dup = seq_parts // width
    piece = length // dup
    own = lax.axis_index("seq")
    chan = own // dup
    half = own % dup
    signal_f = signal.astype(jnp.float32)

    both = jnp.stack([signal_f, long_filter], 1)
    send = jnp.repeat(both, dup, axis=0)
    recv = lax.all_to_all(send, "seq", 0, 0, tiled=True)
    x_rows = recv[:, 0, :]
    h_rows = recv[:, 1, :]

    rows = 2 * seq_parts
    cols = length
    modulus = rows * cols
    row_ids = jnp.arange(rows, dtype=jnp.int32)
    col_ids = jnp.arange(cols, dtype=jnp.int32)
    square = phases(col_ids, col_ids, cols, 1.0)
    turn = phases(row_ids, col_ids, modulus, 1.0)
    square, turn = lax.optimization_barrier((square, turn))
    rows_fwd = (square[0][:, :seq_parts], -square[1][:, :seq_parts])
    turn_fwd = (turn[0], -turn[1])
    cols_fwd = (square[0], -square[1])
    cols_inv = square
    rows_inv = (square[0][:seq_parts], square[1][:seq_parts])

    def forward(x):
        yr, yi = cmat(rows_fwd[0], rows_fwd[1], x, None)
        yr, yi = cmul(yr, yi, turn_fwd[0], turn_fwd[1])
        return cmat(yr, yi, cols_fwd[0], cols_fwd[1])

    xr, xi = forward(x_rows)
    hr, hi = forward(h_rows)
    pr, pi = cmul(xr, xi, hr, hi)
    qr, qi = cmat(pr, pi, cols_inv[0], cols_inv[1])
    qr, qi = cmul(qr, qi, turn_fwd[0], -turn_fwd[1])
    conv = (mat(rows_inv[0], qr) - mat(rows_inv[1], qi)) * (1.0 / modulus)

    skip = lax.dynamic_index_in_dim(skip_weight, chan, keepdims=False)
    mixed = conv + skip * x_rows
    tap_count = short_taps.shape[0]
    taps = lax.dynamic_index_in_dim(short_taps, chan, axis=1, keepdims=False)
    earlier = jnp.concatenate([jnp.zeros((1, length), mixed.dtype), mixed[:-1]], 0)
    joined = jnp.concatenate([mixed, earlier], 1)
    source = jnp.arange(2 * length, dtype=jnp.int32)
    source = jnp.where(source < length, source, source - 2 * length)
    lag = (half * piece + jnp.arange(piece, dtype=jnp.int32))[None, :] - source[:, None]
    band = jnp.zeros(lag.shape, mixed.dtype)
    for offset in range(tap_count):
        band = band + jnp.where(lag == offset, taps[offset], 0.0)
    back = mat(joined, band)
    got = lax.all_to_all(back, "seq", 0, 0, tiled=True)
    short_local = got.reshape(width, length)

    energy = lax.psum(jnp.sum(short_local * short_local, 0), "ch")
    all_channels = width * lax.axis_size("ch")
    return short_local * norm_gain[:, None] * lax.rsqrt(energy / all_channels + 1e-06)[None, :]


def solution(mesh):
    return jax.shard_map(
        local,
        mesh=mesh,
        in_specs=(P("ch", "seq"), P("ch", "seq"), P("ch"), P(None, "ch"), P("ch")),
        out_specs=P("ch", "seq"),
        check_vma=False,
    )
```

```python
import math

import jax
import jax.numpy as jnp
from jax import lax
from jax.sharding import PartitionSpec as P

highest = lax.Precision.HIGH


def phases(left_ids, right_ids, modulus, direction):
    product = left_ids[:, None] * right_ids[None, :] % modulus
    angles = product.astype(jnp.float32) * (2.0 * math.pi / modulus)
    return (jnp.cos(angles), direction * jnp.sin(angles))


def mat(a, b):
    return jnp.dot(a, b, precision=highest, preferred_element_type=jnp.float32)


def cmat(ar, ai, br, bi):
    if ai is None:
        return (mat(ar, br), mat(ar, bi))
    if bi is None:
        return (mat(ar, br), mat(ai, br))
    return (mat(ar, br) - mat(ai, bi), mat(ar, bi) + mat(ai, br))


def cmul(ar, ai, br, bi):
    return (ar * br - ai * bi, ar * bi + ai * br)


def local(signal, long_filter, skip_weight, short_taps, norm_gain):
    seq_parts = lax.axis_size("seq")
    width, length = signal.shape
    dup = seq_parts // width
    piece = length // dup
    own = lax.axis_index("seq")
    chan = own // dup
    half = own % dup
    signal_f = signal.astype(jnp.float32)

    both = jnp.stack([signal_f, long_filter], 1)
    send = jnp.repeat(both, dup, axis=0)
    recv = lax.all_to_all(send, "seq", 0, 0, tiled=True)
    x_rows = recv[:, 0, :]
    h_rows = recv[:, 1, :]

    rows = 2 * seq_parts
    cols = length
    modulus = rows * cols
    row_ids = jnp.arange(rows, dtype=jnp.int32)
    col_ids = jnp.arange(cols, dtype=jnp.int32)
    square = phases(col_ids, col_ids, cols, 1.0)
    turn = phases(row_ids, col_ids, modulus, 1.0)
    square, turn = lax.optimization_barrier((square, turn))
    rows_fwd = (square[0][:, :seq_parts], -square[1][:, :seq_parts])
    turn_fwd = (turn[0], -turn[1])
    cols_fwd = (square[0], -square[1])
    cols_inv = square
    rows_inv = (square[0][:seq_parts], square[1][:seq_parts])

    def forward(x):
        yr, yi = cmat(rows_fwd[0], rows_fwd[1], x, None)
        yr, yi = cmul(yr, yi, turn_fwd[0], turn_fwd[1])
        return cmat(yr, yi, cols_fwd[0], cols_fwd[1])

    xr, xi = forward(x_rows)
    hr, hi = forward(h_rows)
    pr, pi = cmul(xr, xi, hr, hi)
    qr, qi = cmat(pr, pi, cols_inv[0], cols_inv[1])
    qr, qi = cmul(qr, qi, turn_fwd[0], -turn_fwd[1])
    conv = (mat(rows_inv[0], qr) - mat(rows_inv[1], qi)) * (1.0 / modulus)

    skip = lax.dynamic_index_in_dim(skip_weight, chan, keepdims=False)
    mixed = conv + skip * x_rows
    tap_count = short_taps.shape[0]
    taps = lax.dynamic_index_in_dim(short_taps, chan, axis=1, keepdims=False)
    earlier = jnp.concatenate([jnp.zeros((1, length), mixed.dtype), mixed[:-1]], 0)
    joined = jnp.concatenate([mixed, earlier], 1)
    source = jnp.arange(2 * length, dtype=jnp.int32)
    source = jnp.where(source < length, source, source - 2 * length)
    lag = (half * piece + jnp.arange(piece, dtype=jnp.int32))[None, :] - source[:, None]
    band = jnp.zeros(lag.shape, mixed.dtype)
    for offset in range(tap_count):
        band = band + jnp.where(lag == offset, taps[offset], 0.0)
    band = lax.optimization_barrier(band)
    back = mat(joined, band)
    got = lax.all_to_all(back, "seq", 0, 0, tiled=True)
    short_local = got.reshape(width, length)

    energy = lax.psum(jnp.sum(short_local * short_local, 0), "ch")
    all_channels = width * lax.axis_size("ch")
    return short_local * norm_gain[:, None] * lax.rsqrt(energy / all_channels + 1e-06)[None, :]


def solution(mesh):
    return jax.shard_map(
        local,
        mesh=mesh,
        in_specs=(P("ch", "seq"), P("ch", "seq"), P("ch"), P(None, "ch"), P("ch")),
        out_specs=P("ch", "seq"),
        check_vma=False,
    )
```

```python
import math

import jax
import jax.numpy as jnp
from jax import lax
from jax.sharding import PartitionSpec as P

highest = lax.Precision.HIGH


def phases(left_ids, right_ids, modulus, direction):
    product = left_ids[:, None] * right_ids[None, :] % modulus
    angles = product.astype(jnp.float32) * (2.0 * math.pi / modulus)
    return (jnp.cos(angles), direction * jnp.sin(angles))


def mat(a, b):
    return jnp.dot(a, b, precision=highest, preferred_element_type=jnp.float32)


def cmat(ar, ai, br, bi):
    if ai is None:
        return (mat(ar, br), mat(ar, bi))
    if bi is None:
        return (mat(ar, br), mat(ai, br))
    return (mat(ar, br) - mat(ai, bi), mat(ar, bi) + mat(ai, br))


def cmul(ar, ai, br, bi):
    return (ar * br - ai * bi, ar * bi + ai * br)


def local(signal, long_filter, skip_weight, short_taps, norm_gain):
    seq_parts = lax.axis_size("seq")
    width, length = signal.shape
    dup = seq_parts // width
    piece = length // dup
    own = lax.axis_index("seq")
    chan = own // dup
    half = own % dup
    signal_f = signal.astype(jnp.float32)

    both = jnp.stack([signal_f, long_filter], 1)
    send = jnp.repeat(both, dup, axis=0)
    recv = lax.all_to_all(send, "seq", 0, 0, tiled=True)
    x_rows = recv[:, 0, :]
    h_rows = recv[:, 1, :]

    rows = 2 * seq_parts
    cols = length
    modulus = rows * cols
    row_ids = jnp.arange(rows, dtype=jnp.int32)
    col_ids = jnp.arange(cols, dtype=jnp.int32)
    square = phases(col_ids, col_ids, cols, 1.0)
    turn = phases(row_ids, col_ids, modulus, 1.0)
    square, turn = lax.optimization_barrier((square, turn))
    rows_fwd = (square[0][:, :seq_parts], -square[1][:, :seq_parts])
    turn_fwd = (turn[0], -turn[1])
    cols_fwd = (square[0], -square[1])
    cols_inv = square
    rows_inv = (square[0][:seq_parts], square[1][:seq_parts])

    def forward(x):
        yr, yi = cmat(rows_fwd[0], rows_fwd[1], x, None)
        yr, yi = cmul(yr, yi, turn_fwd[0], turn_fwd[1])
        return cmat(yr, yi, cols_fwd[0], cols_fwd[1])

    xr, xi = forward(x_rows)
    hr, hi = forward(h_rows)
    pr, pi = cmul(xr, xi, hr, hi)
    qr, qi = cmat(pr, pi, cols_inv[0], cols_inv[1])
    qr, qi = cmul(qr, qi, turn_fwd[0], -turn_fwd[1])
    conv = (mat(rows_inv[0], qr) - mat(rows_inv[1], qi)) * (1.0 / modulus)

    skip = lax.dynamic_index_in_dim(skip_weight, chan, keepdims=False)
    mixed = conv + skip * x_rows
    tap_count = short_taps.shape[0]
    taps = lax.dynamic_index_in_dim(short_taps, chan, axis=1, keepdims=False)
    earlier = jnp.concatenate([jnp.zeros((1, length), mixed.dtype), mixed[:-1]], 0)
    joined = jnp.concatenate([mixed, earlier], 1)
    source = jnp.arange(2 * length, dtype=jnp.int32)
    source = jnp.where(source < length, source, source - 2 * length)
    lag = (half * piece + jnp.arange(piece, dtype=jnp.int32))[None, :] - source[:, None]
    band = jnp.zeros(lag.shape, mixed.dtype)
    for offset in range(tap_count):
        band = band + jnp.where(lag == offset, taps[offset], 0.0)
    band = lax.optimization_barrier(band)
    back = mat(joined, band)
    got = lax.all_to_all(back, "seq", 0, 0, tiled=True)
    short_local = got.reshape(width, length)

    groups = lax.axis_size("ch")
    partial = jnp.sum(short_local * short_local, 0)
    spread = jnp.broadcast_to(partial[None], (groups,) + partial.shape)
    energy = jnp.sum(lax.all_to_all(spread, "ch", 0, 0, tiled=True), 0)
    all_channels = width * groups
    return short_local * norm_gain[:, None] * lax.rsqrt(energy / all_channels + 1e-06)[None, :]


def solution(mesh):
    return jax.shard_map(
        local,
        mesh=mesh,
        in_specs=(P("ch", "seq"), P("ch", "seq"), P("ch"), P(None, "ch"), P("ch")),
        out_specs=P("ch", "seq"),
        check_vma=False,
    )
```

```python
import math

import jax
import jax.numpy as jnp
from jax import lax
from jax.sharding import PartitionSpec as P

highest = lax.Precision.HIGH


def phases(left_ids, right_ids, modulus, direction):
    product = left_ids[:, None] * right_ids[None, :] % modulus
    angles = product.astype(jnp.float32) * (2.0 * math.pi / modulus)
    return (jnp.cos(angles), direction * jnp.sin(angles))


def mat(a, b):
    return jnp.dot(a, b, precision=highest, preferred_element_type=jnp.float32)


def cmat(ar, ai, br, bi):
    if ai is None:
        return (mat(ar, br), mat(ar, bi))
    if bi is None:
        return (mat(ar, br), mat(ai, br))
    return (mat(ar, br) - mat(ai, bi), mat(ar, bi) + mat(ai, br))


def cmul(ar, ai, br, bi):
    return (ar * br - ai * bi, ar * bi + ai * br)


def local(signal, long_filter, skip_weight, short_taps, norm_gain):
    seq_parts = lax.axis_size("seq")
    width, length = signal.shape
    dup = seq_parts // width
    piece = length // dup
    own = lax.axis_index("seq")
    chan = own // dup
    half = own % dup
    signal_f = signal.astype(jnp.float32)

    both = jnp.stack([signal_f, long_filter], 1)
    mine = lax.all_to_all(both.reshape(seq_parts, length), "seq", 0, 0, tiled=True)
    other = lax.ppermute(mine, "seq", [(i, i ^ 1) for i in range(seq_parts)])
    x_rows = jnp.where(half == 0, mine, other)

    rows = 2 * seq_parts
    cols = length
    modulus = rows * cols
    row_ids = jnp.arange(rows, dtype=jnp.int32)
    col_ids = jnp.arange(cols, dtype=jnp.int32)
    square = phases(col_ids, col_ids, cols, 1.0)
    turn = phases(row_ids, col_ids, modulus, 1.0)
    square, turn = lax.optimization_barrier((square, turn))
    rows_fwd = (square[0][:, :seq_parts], -square[1][:, :seq_parts])
    turn_fwd = (turn[0], -turn[1])
    cols_fwd = (square[0], -square[1])
    cols_inv = square
    rows_inv = (square[0][:seq_parts], square[1][:seq_parts])

    def forward(x):
        yr, yi = cmat(rows_fwd[0], rows_fwd[1], x, None)
        yr, yi = cmul(yr, yi, turn_fwd[0], turn_fwd[1])
        return cmat(yr, yi, cols_fwd[0], cols_fwd[1])

    xr, xi = forward(mine)
    hr, hi = forward(other)
    pr, pi = cmul(xr, xi, hr, hi)
    qr, qi = cmat(pr, pi, cols_inv[0], cols_inv[1])
    qr, qi = cmul(qr, qi, turn_fwd[0], -turn_fwd[1])
    conv = (mat(rows_inv[0], qr) - mat(rows_inv[1], qi)) * (1.0 / modulus)

    skip = lax.dynamic_index_in_dim(skip_weight, chan, keepdims=False)
    mixed = conv + skip * x_rows
    tap_count = short_taps.shape[0]
    taps = lax.dynamic_index_in_dim(short_taps, chan, axis=1, keepdims=False)
    earlier = jnp.concatenate([jnp.zeros((1, length), mixed.dtype), mixed[:-1]], 0)
    joined = jnp.concatenate([mixed, earlier], 1)
    source = jnp.arange(2 * length, dtype=jnp.int32)
    source = jnp.where(source < length, source, source - 2 * length)
    lag = (half * piece + jnp.arange(piece, dtype=jnp.int32))[None, :] - source[:, None]
    band = jnp.zeros(lag.shape, mixed.dtype)
    for offset in range(tap_count):
        band = band + jnp.where(lag == offset, taps[offset], 0.0)
    band = lax.optimization_barrier(band)
    back = mat(joined, band)
    got = lax.all_to_all(back, "seq", 0, 0, tiled=True)
    short_local = got.reshape(width, length)

    groups = lax.axis_size("ch")
    partial = jnp.sum(short_local * short_local, 0)
    spread = jnp.broadcast_to(partial[None], (groups,) + partial.shape)
    energy = jnp.sum(lax.all_to_all(spread, "ch", 0, 0, tiled=True), 0)
    all_channels = width * groups
    return short_local * norm_gain[:, None] * lax.rsqrt(energy / all_channels + 1e-06)[None, :]


def solution(mesh):
    return jax.shard_map(
        local,
        mesh=mesh,
        in_specs=(P("ch", "seq"), P("ch", "seq"), P("ch"), P(None, "ch"), P("ch")),
        out_specs=P("ch", "seq"),
        check_vma=False,
    )
```

```python
import math

import jax
import jax.numpy as jnp
from jax import lax
from jax.sharding import PartitionSpec as P

highest = lax.Precision.HIGH


def phases(left_ids, right_ids, modulus, direction):
    product = left_ids[:, None] * right_ids[None, :] % modulus
    angles = product.astype(jnp.float32) * (2.0 * math.pi / modulus)
    return (jnp.cos(angles), direction * jnp.sin(angles))


def mat(a, b):
    return jnp.dot(a, b, precision=highest, preferred_element_type=jnp.float32)


def cmat(ar, ai, br, bi):
    if ai is None:
        return (mat(ar, br), mat(ar, bi))
    if bi is None:
        return (mat(ar, br), mat(ai, br))
    return (mat(ar, br) - mat(ai, bi), mat(ar, bi) + mat(ai, br))


def gauss(ar, ai, table):
    br, bsum, bdiff = table
    common = mat(ar + ai, br)
    return (common - mat(ai, bsum), common + mat(ar, bdiff))


def with_sums(br, bi):
    return (br, br + bi, bi - br)


def cmul(ar, ai, br, bi):
    return (ar * br - ai * bi, ar * bi + ai * br)


def local(signal, long_filter, skip_weight, short_taps, norm_gain):
    seq_parts = lax.axis_size("seq")
    width, length = signal.shape
    dup = seq_parts // width
    piece = length // dup
    own = lax.axis_index("seq")
    chan = own // dup
    half = own % dup
    signal_f = signal.astype(jnp.float32)

    both = jnp.stack([signal_f, long_filter], 1)
    mine = lax.all_to_all(both.reshape(seq_parts, length), "seq", 0, 0, tiled=True)
    other = lax.ppermute(mine, "seq", [(i, i ^ 1) for i in range(seq_parts)])
    x_rows = jnp.where(half == 0, mine, other)

    rows = 2 * seq_parts
    cols = length
    modulus = rows * cols
    row_ids = jnp.arange(rows, dtype=jnp.int32)
    col_ids = jnp.arange(cols, dtype=jnp.int32)
    square = phases(col_ids, col_ids, cols, 1.0)
    turn = phases(row_ids, col_ids, modulus, 1.0)
    cols_fwd = with_sums(square[0], -square[1])
    cols_inv = with_sums(square[0], square[1])
    square, turn, cols_fwd, cols_inv = lax.optimization_barrier((square, turn, cols_fwd, cols_inv))
    rows_fwd = (square[0][:, :seq_parts], -square[1][:, :seq_parts])
    turn_fwd = (turn[0], -turn[1])
    rows_inv = (square[0][:seq_parts], square[1][:seq_parts])

    def forward(x):
        yr, yi = cmat(rows_fwd[0], rows_fwd[1], x, None)
        yr, yi = cmul(yr, yi, turn_fwd[0], turn_fwd[1])
        return gauss(yr, yi, cols_fwd)

    xr, xi = forward(mine)
    hr, hi = forward(other)
    pr, pi = cmul(xr, xi, hr, hi)
    qr, qi = gauss(pr, pi, cols_inv)
    qr, qi = cmul(qr, qi, turn_fwd[0], -turn_fwd[1])
    conv = (mat(rows_inv[0], qr) - mat(rows_inv[1], qi)) * (1.0 / modulus)

    skip = lax.dynamic_index_in_dim(skip_weight, chan, keepdims=False)
    mixed = conv + skip * x_rows
    tap_count = short_taps.shape[0]
    taps = lax.dynamic_index_in_dim(short_taps, chan, axis=1, keepdims=False)
    earlier = jnp.concatenate([jnp.zeros((1, length), mixed.dtype), mixed[:-1]], 0)
    joined = jnp.concatenate([mixed, earlier], 1)
    source = jnp.arange(2 * length, dtype=jnp.int32)
    source = jnp.where(source < length, source, source - 2 * length)
    lag = (half * piece + jnp.arange(piece, dtype=jnp.int32))[None, :] - source[:, None]
    band = jnp.zeros(lag.shape, mixed.dtype)
    for offset in range(tap_count):
        band = band + jnp.where(lag == offset, taps[offset], 0.0)
    band = lax.optimization_barrier(band)
    back = mat(joined, band)
    got = lax.all_to_all(back, "seq", 0, 0, tiled=True)
    short_local = got.reshape(width, length)

    groups = lax.axis_size("ch")
    partial = jnp.sum(short_local * short_local, 0)
    spread = jnp.broadcast_to(partial[None], (groups,) + partial.shape)
    energy = jnp.sum(lax.all_to_all(spread, "ch", 0, 0, tiled=True), 0)
    all_channels = width * groups
    return short_local * norm_gain[:, None] * lax.rsqrt(energy / all_channels + 1e-06)[None, :]


def solution(mesh):
    return jax.shard_map(
        local,
        mesh=mesh,
        in_specs=(P("ch", "seq"), P("ch", "seq"), P("ch"), P(None, "ch"), P("ch")),
        out_specs=P("ch", "seq"),
        check_vma=False,
    )
```

```python
import math

import jax
import jax.numpy as jnp
from jax import lax
from jax.sharding import PartitionSpec as P

highest = lax.Precision.HIGH


def phases(left_ids, right_ids, modulus, direction):
    product = left_ids[:, None] * right_ids[None, :] % modulus
    angles = product.astype(jnp.float32) * (2.0 * math.pi / modulus)
    return (jnp.cos(angles), direction * jnp.sin(angles))


def mat(a, b):
    return jnp.dot(a, b, precision=highest, preferred_element_type=jnp.float32)


def cmat(ar, ai, br, bi):
    if ai is None:
        return (mat(ar, br), mat(ar, bi))
    if bi is None:
        return (mat(ar, br), mat(ai, br))
    return (mat(ar, br) - mat(ai, bi), mat(ar, bi) + mat(ai, br))


def cmul(ar, ai, br, bi):
    return (ar * br - ai * bi, ar * bi + ai * br)


def local(signal, long_filter, skip_weight, short_taps, norm_gain):
    seq_parts = lax.axis_size("seq")
    width, length = signal.shape
    dup = seq_parts // width
    piece = length // dup
    own = lax.axis_index("seq")
    chan = own // dup
    half = own % dup
    signal_f = signal.astype(jnp.float32)
    gains = jnp.broadcast_to(norm_gain[:, None], signal.shape)
    gains, signal_f = lax.optimization_barrier((gains, signal_f))

    both = jnp.stack([signal_f, long_filter], 1)
    mine = lax.all_to_all(both.reshape(seq_parts, length), "seq", 0, 0, tiled=True)
    other = lax.ppermute(mine, "seq", [(i, i ^ 1) for i in range(seq_parts)])
    x_rows = jnp.where(half == 0, mine, other)

    rows = 2 * seq_parts
    cols = length
    modulus = rows * cols
    row_ids = jnp.arange(rows, dtype=jnp.int32)
    col_ids = jnp.arange(cols, dtype=jnp.int32)
    square = phases(col_ids, col_ids, cols, 1.0)
    turn = phases(row_ids, col_ids, modulus, 1.0)
    square, turn = lax.optimization_barrier((square, turn))
    rows_fwd = (square[0][:, :seq_parts], -square[1][:, :seq_parts])
    turn_fwd = (turn[0], -turn[1])
    cols_fwd = (square[0], -square[1])
    cols_inv = square
    rows_inv = (square[0][:seq_parts], square[1][:seq_parts])

    def forward(x):
        yr, yi = cmat(rows_fwd[0], rows_fwd[1], x, None)
        yr, yi = cmul(yr, yi, turn_fwd[0], turn_fwd[1])
        return cmat(yr, yi, cols_fwd[0], cols_fwd[1])

    xr, xi = forward(mine)
    hr, hi = forward(other)
    pr, pi = cmul(xr, xi, hr, hi)
    qr, qi = cmat(pr, pi, cols_inv[0], cols_inv[1])
    qr, qi = cmul(qr, qi, turn_fwd[0], -turn_fwd[1])
    conv = (mat(rows_inv[0], qr) - mat(rows_inv[1], qi)) * (1.0 / modulus)

    skip = lax.dynamic_index_in_dim(skip_weight, chan, keepdims=False)
    mixed = conv + skip * x_rows
    tap_count = short_taps.shape[0]
    taps = lax.dynamic_index_in_dim(short_taps, chan, axis=1, keepdims=False)
    earlier = jnp.concatenate([jnp.zeros((1, length), mixed.dtype), mixed[:-1]], 0)
    joined = jnp.concatenate([mixed, earlier], 1)
    source = jnp.arange(2 * length, dtype=jnp.int32)
    source = jnp.where(source < length, source, source - 2 * length)
    lag = (half * piece + jnp.arange(piece, dtype=jnp.int32))[None, :] - source[:, None]
    band = jnp.zeros(lag.shape, mixed.dtype)
    for offset in range(tap_count):
        band = band + jnp.where(lag == offset, taps[offset], 0.0)
    band = lax.optimization_barrier(band)
    back = mat(joined, band)
    got = lax.all_to_all(back, "seq", 0, 0, tiled=True)
    short_local = got.reshape(width, length)

    groups = lax.axis_size("ch")
    partial = jnp.sum(short_local * short_local, 0)
    spread = jnp.broadcast_to(partial[None], (groups,) + partial.shape)
    energy = jnp.sum(lax.all_to_all(spread, "ch", 0, 0, tiled=True), 0)
    all_channels = width * groups
    return short_local * gains * lax.rsqrt(energy / all_channels + 1e-06)[None, :]


def solution(mesh):
    return jax.shard_map(
        local,
        mesh=mesh,
        in_specs=(P("ch", "seq"), P("ch", "seq"), P("ch"), P(None, "ch"), P("ch")),
        out_specs=P("ch", "seq"),
        check_vma=False,
    )
```

```python
import math

import jax
import jax.numpy as jnp
from jax import lax
from jax.sharding import PartitionSpec as P

highest = lax.Precision.HIGH


def phases(left_ids, right_ids, modulus, direction):
    product = left_ids[:, None] * right_ids[None, :] % modulus
    angles = product.astype(jnp.float32) * (2.0 * math.pi / modulus)
    return (jnp.cos(angles), direction * jnp.sin(angles))


def mat(a, b):
    return jnp.dot(a, b, precision=highest, preferred_element_type=jnp.float32)


def cmat(ar, ai, br, bi):
    if ai is None:
        return (mat(ar, br), mat(ar, bi))
    if bi is None:
        return (mat(ar, br), mat(ai, br))
    return (mat(ar, br) - mat(ai, bi), mat(ar, bi) + mat(ai, br))


def cmul(ar, ai, br, bi):
    return (ar * br - ai * bi, ar * bi + ai * br)


def local(signal, long_filter, skip_weight, short_taps, norm_gain):
    seq_parts = lax.axis_size("seq")
    width, length = signal.shape
    dup = seq_parts // width
    piece = length // dup
    own = lax.axis_index("seq")
    chan = own // dup
    half = own % dup
    signal_f = signal.astype(jnp.float32)
    gains = jnp.broadcast_to(norm_gain[:, None], signal.shape)
    gains, signal_f = lax.optimization_barrier((gains, signal_f))

    both = jnp.stack([signal_f, long_filter], 1)
    mine = lax.all_to_all(both.reshape(seq_parts, length), "seq", 0, 0, tiled=True)
    other = lax.ppermute(mine, "seq", [(i, i ^ 1) for i in range(seq_parts)])
    x_rows = jnp.where(half == 0, mine, other)

    rows = 2 * seq_parts
    cols = length
    modulus = rows * cols
    row_ids = jnp.arange(rows, dtype=jnp.int32)
    col_ids = jnp.arange(cols, dtype=jnp.int32)
    square = phases(col_ids, col_ids, cols, 1.0)
    turn = phases(row_ids, col_ids, modulus, 1.0)
    square, turn = lax.optimization_barrier((square, turn))
    rows_fwd = (square[0][:, :seq_parts], -square[1][:, :seq_parts])
    turn_fwd = (turn[0], -turn[1])
    cols_fwd = (square[0], -square[1])
    cols_inv = square
    rows_inv = (square[0][:seq_parts], square[1][:seq_parts])

    def forward(x):
        yr, yi = cmat(rows_fwd[0], rows_fwd[1], x, None)
        yr, yi = cmul(yr, yi, turn_fwd[0], turn_fwd[1])
        return cmat(yr, yi, cols_fwd[0], cols_fwd[1])

    xr, xi = forward(mine)
    hr, hi = forward(other)
    pr, pi = cmul(xr, xi, hr, hi)
    qr, qi = cmat(pr, pi, cols_inv[0], cols_inv[1])
    qr, qi = cmul(qr, qi, turn_fwd[0], -turn_fwd[1])
    conv = (mat(rows_inv[0], qr) - mat(rows_inv[1], qi)) * (1.0 / modulus)

    skip = lax.dynamic_index_in_dim(skip_weight, chan, keepdims=False)
    mixed = conv + skip * x_rows
    tap_count = short_taps.shape[0]
    taps = lax.dynamic_index_in_dim(short_taps, chan, axis=1, keepdims=False)
    earlier = jnp.concatenate([jnp.zeros((1, length), mixed.dtype), mixed[:-1]], 0)
    joined = jnp.concatenate([mixed, earlier], 1)
    source = jnp.arange(2 * length, dtype=jnp.int32)
    source = jnp.where(source < length, source, source - 2 * length)
    lag = (half * piece + jnp.arange(piece, dtype=jnp.int32))[None, :] - source[:, None]
    band = jnp.zeros(lag.shape, mixed.dtype)
    for offset in range(tap_count):
        band = band + jnp.where(lag == offset, taps[offset], 0.0)
    band = lax.optimization_barrier(band)
    back = mat(joined, band)
    got = lax.all_to_all(back, "seq", 0, 0, tiled=True)
    short_local = got.reshape(width, length)

    groups = lax.axis_size("ch")
    folded = got.reshape(width, dup, piece)
    partial = jnp.sum(folded * folded, 0).reshape(length)
    spread = jnp.broadcast_to(partial[None], (groups,) + partial.shape)
    energy = jnp.sum(lax.all_to_all(spread, "ch", 0, 0, tiled=True), 0)
    all_channels = width * groups
    return short_local * gains * lax.rsqrt(energy / all_channels + 1e-06)[None, :]


def solution(mesh):
    return jax.shard_map(
        local,
        mesh=mesh,
        in_specs=(P("ch", "seq"), P("ch", "seq"), P("ch"), P(None, "ch"), P("ch")),
        out_specs=P("ch", "seq"),
        check_vma=False,
    )
```

```python
import math

import jax
import jax.numpy as jnp
from jax import lax
from jax.sharding import PartitionSpec as P

highest = lax.Precision.HIGH


def phases(left_ids, right_ids, modulus, direction):
    product = left_ids[:, None] * right_ids[None, :] % modulus
    angles = product.astype(jnp.float32) * (2.0 * math.pi / modulus)
    return (jnp.cos(angles), direction * jnp.sin(angles))


def mat(a, b):
    return jnp.dot(a, b, precision=highest, preferred_element_type=jnp.float32)


def cmat(ar, ai, br, bi):
    if ai is None:
        return (mat(ar, br), mat(ar, bi))
    if bi is None:
        return (mat(ar, br), mat(ai, br))
    return (mat(ar, br) - mat(ai, bi), mat(ar, bi) + mat(ai, br))


def cmul(ar, ai, br, bi):
    return (ar * br - ai * bi, ar * bi + ai * br)


def local(signal, long_filter, skip_weight, short_taps, norm_gain):
    chips = lax.axis_size("chip")
    width, length = signal.shape
    chan = lax.axis_index("chip")
    half = lax.axis_index("core")
    signal_f = signal.astype(jnp.float32)
    gains = jnp.broadcast_to(norm_gain[:, None], signal.shape)
    gains, signal_f = lax.optimization_barrier((gains, signal_f))

    both = jnp.stack([signal_f, long_filter], 1)
    mine = lax.all_to_all(both, "chip", 0, 0, tiled=True)
    other = lax.ppermute(mine, "core", [(0, 1), (1, 0)])

    seq_parts = 2 * chips
    rows = 2 * seq_parts
    cols = length
    modulus = rows * cols
    row_ids = jnp.arange(rows, dtype=jnp.int32)
    col_ids = jnp.arange(cols, dtype=jnp.int32)
    chip_ids = jnp.arange(chips, dtype=jnp.int32)
    square = phases(col_ids, col_ids, cols, 1.0)
    turn = phases(row_ids, col_ids, modulus, 1.0)
    rows_mine = phases(row_ids, 2 * chip_ids + half, rows, -1.0)
    rows_other = phases(row_ids, 2 * chip_ids + 1 - half, rows, -1.0)
    parity_ids = jnp.concatenate([2 * chip_ids, 2 * chip_ids + 1])
    rows_inv = phases(parity_ids, row_ids, rows, 1.0)
    square, turn, rows_mine, rows_other, rows_inv = lax.optimization_barrier(
        (square, turn, rows_mine, rows_other, rows_inv)
    )
    turn_fwd = (turn[0], -turn[1])
    cols_fwd = (square[0], -square[1])
    cols_inv = square

    def forward(own_rows, other_rows):
        yr = mat(rows_mine[0], own_rows) + mat(rows_other[0], other_rows)
        yi = mat(rows_mine[1], own_rows) + mat(rows_other[1], other_rows)
        yr, yi = cmul(yr, yi, turn_fwd[0], turn_fwd[1])
        return cmat(yr, yi, cols_fwd[0], cols_fwd[1])

    xr, xi = forward(mine[:, 0], other[:, 0])
    hr, hi = forward(mine[:, 1], other[:, 1])
    pr, pi = cmul(xr, xi, hr, hi)
    qr, qi = cmat(pr, pi, cols_inv[0], cols_inv[1])
    qr, qi = cmul(qr, qi, turn_fwd[0], -turn_fwd[1])
    conv = (mat(rows_inv[0], qr) - mat(rows_inv[1], qi)) * (1.0 / modulus)

    first = half == 0
    x_rows = jnp.where(
        first,
        jnp.concatenate([mine[:, 0], other[:, 0]], 0),
        jnp.concatenate([other[:, 0], mine[:, 0]], 0),
    )
    skip = lax.dynamic_index_in_dim(skip_weight, chan, keepdims=False)
    mixed = conv + skip * x_rows
    tap_count = short_taps.shape[0]
    taps = lax.dynamic_index_in_dim(short_taps, chan, axis=1, keepdims=False)
    even, odd = mixed[:chips], mixed[chips:]
    own_rows = jnp.where(first, even, odd)
    odd_before = jnp.concatenate([jnp.zeros((1, length), mixed.dtype), odd[:-1]], 0)
    earlier = jnp.where(first, odd_before, even)
    joined = jnp.concatenate([own_rows, earlier], 1)
    source = jnp.arange(2 * length, dtype=jnp.int32)
    source = jnp.where(source < length, source, source - 2 * length)
    lag = col_ids[None, :] - source[:, None]
    band = jnp.zeros(lag.shape, mixed.dtype)
    for offset in range(tap_count):
        band = band + jnp.where(lag == offset, taps[offset], 0.0)
    band = lax.optimization_barrier(band)
    back = mat(joined, band)
    short_local = lax.all_to_all(back, "chip", 0, 0, tiled=True)

    groups = lax.axis_size("ch")
    partial = jnp.sum(short_local * short_local, 0)
    spread = jnp.broadcast_to(partial[None], (groups,) + partial.shape)
    energy = jnp.sum(lax.all_to_all(spread, "ch", 0, 0, tiled=True), 0)
    all_channels = width * groups
    return short_local * gains * lax.rsqrt(energy / all_channels + 1e-06)[None, :]


def solution(mesh):
    seq_parts, groups = mesh.devices.shape
    split = jax.sharding.Mesh(mesh.devices.reshape(seq_parts // 2, 2, groups), ("chip", "core", "ch"))
    seq = ("chip", "core")
    return jax.shard_map(
        local,
        mesh=split,
        in_specs=(P("ch", seq), P("ch", seq), P("ch"), P(None, "ch"), P("ch")),
        out_specs=P("ch", seq),
        check_vma=False,
    )
```

```python
import math

import jax
import jax.numpy as jnp
from jax import lax
from jax.sharding import PartitionSpec as P

highest = lax.Precision.HIGH


def phases(left_ids, right_ids, modulus, direction):
    product = left_ids[:, None] * right_ids[None, :] % modulus
    angles = product.astype(jnp.float32) * (2.0 * math.pi / modulus)
    return (jnp.cos(angles), direction * jnp.sin(angles))


def mat(a, b):
    return jnp.dot(a, b, precision=highest, preferred_element_type=jnp.float32)


def cmat(ar, ai, br, bi):
    if ai is None:
        return (mat(ar, br), mat(ar, bi))
    if bi is None:
        return (mat(ar, br), mat(ai, br))
    return (mat(ar, br) - mat(ai, bi), mat(ar, bi) + mat(ai, br))


def cmul(ar, ai, br, bi):
    return (ar * br - ai * bi, ar * bi + ai * br)


def local(signal, long_filter, skip_weight, short_taps, norm_gain):
    chips = lax.axis_size("chip")
    width, length = signal.shape
    chan = lax.axis_index("chip")
    half = lax.axis_index("core")
    signal_f = signal.astype(jnp.float32)
    gains = jnp.broadcast_to(norm_gain[:, None], signal.shape)
    gains, signal_f = lax.optimization_barrier((gains, signal_f))

    both = jnp.stack([signal_f, long_filter], 1)
    mine = lax.all_to_all(both, "chip", 0, 0, tiled=True)
    other = lax.ppermute(mine, "core", [(0, 1), (1, 0)])

    seq_parts = 2 * chips
    rows = 2 * seq_parts
    cols = length
    modulus = rows * cols
    row_ids = jnp.arange(rows, dtype=jnp.int32)
    col_ids = jnp.arange(cols, dtype=jnp.int32)
    chip_ids = jnp.arange(chips, dtype=jnp.int32)
    square = phases(col_ids, col_ids, cols, 1.0)
    turn = phases(row_ids, col_ids, modulus, 1.0)
    rows_mine = phases(row_ids, 2 * chip_ids + half, rows, -1.0)
    rows_other = phases(row_ids, 2 * chip_ids + 1 - half, rows, -1.0)
    rows_back = phases(2 * chip_ids + half, row_ids, rows, 1.0)
    tap_count = short_taps.shape[0]
    tap_ids = jnp.arange(tap_count, dtype=jnp.int32)
    taps = lax.dynamic_index_in_dim(short_taps, chan, axis=1, keepdims=False)
    tap_rows = phases(row_ids, tap_ids, modulus, -1.0)
    tap_cols = phases(tap_ids, col_ids, cols, -1.0)
    tap_spec = cmat(taps[None, :] * tap_rows[0], taps[None, :] * tap_rows[1], tap_cols[0], tap_cols[1])
    square, turn, rows_mine, rows_other, rows_back, tap_spec = lax.optimization_barrier(
        (square, turn, rows_mine, rows_other, rows_back, tap_spec)
    )
    turn_fwd = (turn[0], -turn[1])
    cols_fwd = (square[0], -square[1])
    cols_inv = square

    def forward(own_rows, other_rows):
        yr = mat(rows_mine[0], own_rows) + mat(rows_other[0], other_rows)
        yi = mat(rows_mine[1], own_rows) + mat(rows_other[1], other_rows)
        yr, yi = cmul(yr, yi, turn_fwd[0], turn_fwd[1])
        return cmat(yr, yi, cols_fwd[0], cols_fwd[1])

    skip = lax.dynamic_index_in_dim(skip_weight, chan, keepdims=False)
    xr, xi = forward(mine[:, 0], other[:, 0])
    hr, hi = forward(mine[:, 1], other[:, 1])
    pr, pi = cmul(xr, xi, hr + skip, hi)
    pr, pi = cmul(pr, pi, tap_spec[0], tap_spec[1])
    qr, qi = cmat(pr, pi, cols_inv[0], cols_inv[1])
    qr, qi = cmul(qr, qi, turn_fwd[0], -turn_fwd[1])
    back = (mat(rows_back[0], qr) - mat(rows_back[1], qi)) * (1.0 / modulus)

    last = jnp.where(half == 1, mine[chips - 1], other[chips - 1])
    rim = tap_count - 2
    x_end = last[0, length - rim :][::-1]
    h_end = last[1, length - rim :][::-1]
    wrapped = [sum(x_end[i] * h_end[q - i] for i in range(q + 1)) for q in range(rim)]
    wrap = [
        sum(taps[t + r] * wrapped[r - 2] for r in range(2, tap_count - t)) for t in range(rim)
    ]
    fix = jnp.stack(wrap) * (half == 0).astype(back.dtype)
    back = back.at[0, :rim].add(-fix)
    short_local = lax.all_to_all(back, "chip", 0, 0, tiled=True)

    groups = lax.axis_size("ch")
    partial = jnp.sum(short_local * short_local, 0)
    spread = jnp.broadcast_to(partial[None], (groups,) + partial.shape)
    energy = jnp.sum(lax.all_to_all(spread, "ch", 0, 0, tiled=True), 0)
    all_channels = width * groups
    return short_local * gains * lax.rsqrt(energy / all_channels + 1e-06)[None, :]


def solution(mesh):
    seq_parts, groups = mesh.devices.shape
    split = jax.sharding.Mesh(mesh.devices.reshape(seq_parts // 2, 2, groups), ("chip", "core", "ch"))
    seq = ("chip", "core")
    return jax.shard_map(
        local,
        mesh=split,
        in_specs=(P("ch", seq), P("ch", seq), P("ch"), P(None, "ch"), P("ch")),
        out_specs=P("ch", seq),
        check_vma=False,
    )
```

```python
import math

import jax
import jax.numpy as jnp
from jax import lax
from jax.sharding import PartitionSpec as P

highest = lax.Precision.HIGH


def phases(left_ids, right_ids, modulus, direction):
    product = left_ids[:, None] * right_ids[None, :] % modulus
    angles = product.astype(jnp.float32) * (2.0 * math.pi / modulus)
    return (jnp.cos(angles), direction * jnp.sin(angles))


def mat(a, b):
    return jnp.dot(a, b, precision=highest, preferred_element_type=jnp.float32)


def cmat(ar, ai, br, bi):
    if ai is None:
        return (mat(ar, br), mat(ar, bi))
    if bi is None:
        return (mat(ar, br), mat(ai, br))
    return (mat(ar, br) - mat(ai, bi), mat(ar, bi) + mat(ai, br))


def cmul(ar, ai, br, bi):
    return (ar * br - ai * bi, ar * bi + ai * br)


def local(signal, long_filter, skip_weight, short_taps, norm_gain):
    chips = lax.axis_size("chip")
    width, length = signal.shape
    chan = lax.axis_index("chip")
    half = lax.axis_index("core")
    signal_f = signal.astype(jnp.float32)
    gains = jnp.broadcast_to(norm_gain[:, None], signal.shape)
    gains, signal_f = lax.optimization_barrier((gains, signal_f))

    both = jnp.stack([signal_f, long_filter], 1)
    mine = lax.all_to_all(both, "chip", 0, 0, tiled=True)
    other = lax.ppermute(mine, "core", [(0, 1), (1, 0)])

    seq_parts = 2 * chips
    rows = 2 * seq_parts
    cols = length
    modulus = rows * cols
    row_ids = jnp.arange(rows, dtype=jnp.int32)
    col_ids = jnp.arange(cols, dtype=jnp.int32)
    chip_ids = jnp.arange(chips, dtype=jnp.int32)
    square = phases(col_ids, col_ids, cols, 1.0)
    turn = phases(row_ids, col_ids, modulus, 1.0)
    rows_mine = phases(row_ids, 2 * chip_ids + half, rows, -1.0)
    rows_other = phases(row_ids, 2 * chip_ids + 1 - half, rows, -1.0)
    rows_back = phases(2 * chip_ids + half, row_ids, rows, 1.0)
    tap_count = short_taps.shape[0]
    tap_ids = jnp.arange(tap_count, dtype=jnp.int32)
    taps = lax.dynamic_index_in_dim(short_taps, chan, axis=1, keepdims=False)
    tap_rows = phases(row_ids, tap_ids, modulus, -1.0)
    tap_cols = phases(tap_ids, col_ids, cols, -1.0)
    tap_spec = cmat(taps[None, :] * tap_rows[0], taps[None, :] * tap_rows[1], tap_cols[0], tap_cols[1])
    square, turn, rows_mine, rows_other, rows_back, tap_spec = lax.optimization_barrier(
        (square, turn, rows_mine, rows_other, rows_back, tap_spec)
    )
    turn_fwd = (turn[0], -turn[1])
    cols_fwd = (square[0], -square[1])
    cols_inv = square

    def forward(own_rows, other_rows):
        yr = mat(rows_mine[0], own_rows) + mat(rows_other[0], other_rows)
        yi = mat(rows_mine[1], own_rows) + mat(rows_other[1], other_rows)
        yr, yi = cmul(yr, yi, turn_fwd[0], turn_fwd[1])
        return cmat(yr, yi, cols_fwd[0], cols_fwd[1])

    skip = lax.dynamic_index_in_dim(skip_weight, chan, keepdims=False)
    xr, xi = forward(mine[:, 0], other[:, 0])
    hr, hi = forward(mine[:, 1], other[:, 1])
    pr, pi = cmul(xr, xi, hr + skip, hi)
    pr, pi = cmul(pr, pi, tap_spec[0], tap_spec[1])
    qr, qi = cmat(pr, pi, cols_inv[0], cols_inv[1])
    qr, qi = cmul(qr, qi, turn_fwd[0], -turn_fwd[1])
    back = (mat(rows_back[0], qr) - mat(rows_back[1], qi)) * (1.0 / modulus)

    last = jnp.where(half == 1, mine[chips - 1], other[chips - 1])
    rim = tap_count - 2
    x_end = last[0, length - rim :][::-1]
    h_end = last[1, length - rim :][::-1]
    near = jnp.arange(rim, dtype=jnp.int32)
    pair_sum = near[:, None, None] + near[None, :, None]
    wrapped = jnp.sum(
        jnp.where(pair_sum == near[None, None, :], x_end[:, None, None] * h_end[None, :, None], 0.0),
        (0, 1),
    )
    reach = pair_sum[:, :, 0] + 2
    weights = jnp.zeros((rim, rim), taps.dtype)
    for offset in range(2, tap_count):
        weights = weights + jnp.where(reach == offset, taps[offset], 0.0)
    wrap = jnp.sum(weights * wrapped[None, :], 1)
    fix = wrap * (half == 0).astype(back.dtype)
    back = back.at[0, :rim].add(-fix)
    short_local = lax.all_to_all(back, "chip", 0, 0, tiled=True)

    groups = lax.axis_size("ch")
    partial = jnp.sum(short_local * short_local, 0)
    spread = jnp.broadcast_to(partial[None], (groups,) + partial.shape)
    energy = jnp.sum(lax.all_to_all(spread, "ch", 0, 0, tiled=True), 0)
    all_channels = width * groups
    return short_local * gains * lax.rsqrt(energy / all_channels + 1e-06)[None, :]


def solution(mesh):
    seq_parts, groups = mesh.devices.shape
    split = jax.sharding.Mesh(mesh.devices.reshape(seq_parts // 2, 2, groups), ("chip", "core", "ch"))
    seq = ("chip", "core")
    return jax.shard_map(
        local,
        mesh=split,
        in_specs=(P("ch", seq), P("ch", seq), P("ch"), P(None, "ch"), P("ch")),
        out_specs=P("ch", seq),
        check_vma=False,
    )
```

```python
import math

import jax
import jax.numpy as jnp
from jax import lax
from jax.sharding import PartitionSpec as P

highest = lax.Precision.HIGH


def phases(left_ids, right_ids, modulus, direction):
    product = left_ids[:, None] * right_ids[None, :] % modulus
    angles = product.astype(jnp.float32) * (2.0 * math.pi / modulus)
    return (jnp.cos(angles), direction * jnp.sin(angles))


def mat(a, b):
    return jnp.dot(a, b, precision=highest, preferred_element_type=jnp.float32)


def cmat(ar, ai, br, bi):
    if ai is None:
        return (mat(ar, br), mat(ar, bi))
    if bi is None:
        return (mat(ar, br), mat(ai, br))
    return (mat(ar, br) - mat(ai, bi), mat(ar, bi) + mat(ai, br))


def gauss(ar, ai, table):
    br, bsum, bdiff = table
    common = mat(ar + ai, br)
    return (common - mat(ai, bsum), common + mat(ar, bdiff))


def with_sums(br, bi):
    return (br, br + bi, bi - br)


def cmul(ar, ai, br, bi):
    return (ar * br - ai * bi, ar * bi + ai * br)


def local(signal, long_filter, skip_weight, short_taps, norm_gain):
    chips = lax.axis_size("chip")
    width, length = signal.shape
    chan = lax.axis_index("chip")
    half = lax.axis_index("core")
    signal_f = signal.astype(jnp.float32)
    gains = jnp.broadcast_to(norm_gain[:, None], signal.shape)
    gains, signal_f = lax.optimization_barrier((gains, signal_f))

    both = jnp.stack([signal_f, long_filter], 1)
    mine = lax.all_to_all(both, "chip", 0, 0, tiled=True)
    other = lax.ppermute(mine, "core", [(0, 1), (1, 0)])

    seq_parts = 2 * chips
    rows = 2 * seq_parts
    cols = length
    modulus = rows * cols
    row_ids = jnp.arange(rows, dtype=jnp.int32)
    col_ids = jnp.arange(cols, dtype=jnp.int32)
    chip_ids = jnp.arange(chips, dtype=jnp.int32)
    square = phases(col_ids, col_ids, cols, 1.0)
    turn = phases(row_ids, col_ids, modulus, 1.0)
    rows_mine = phases(row_ids, 2 * chip_ids + half, rows, -1.0)
    rows_other = phases(row_ids, 2 * chip_ids + 1 - half, rows, -1.0)
    parity_ids = jnp.concatenate([2 * chip_ids, 2 * chip_ids + 1])
    rows_inv = phases(parity_ids, row_ids, rows, 1.0)
    cols_fwd = with_sums(square[0], -square[1])
    cols_inv = with_sums(square[0], square[1])
    square, turn, rows_mine, rows_other, rows_inv, cols_fwd, cols_inv = lax.optimization_barrier(
        (square, turn, rows_mine, rows_other, rows_inv, cols_fwd, cols_inv)
    )
    turn_fwd = (turn[0], -turn[1])

    def forward(own_rows, other_rows):
        yr = mat(rows_mine[0], own_rows) + mat(rows_other[0], other_rows)
        yi = mat(rows_mine[1], own_rows) + mat(rows_other[1], other_rows)
        yr, yi = cmul(yr, yi, turn_fwd[0], turn_fwd[1])
        return gauss(yr, yi, cols_fwd)

    xr, xi = forward(mine[:, 0], other[:, 0])
    hr, hi = forward(mine[:, 1], other[:, 1])
    pr, pi = cmul(xr, xi, hr, hi)
    qr, qi = gauss(pr, pi, cols_inv)
    qr, qi = cmul(qr, qi, turn_fwd[0], -turn_fwd[1])
    conv = (mat(rows_inv[0], qr) - mat(rows_inv[1], qi)) * (1.0 / modulus)

    first = half == 0
    x_rows = jnp.where(
        first,
        jnp.concatenate([mine[:, 0], other[:, 0]], 0),
        jnp.concatenate([other[:, 0], mine[:, 0]], 0),
    )
    skip = lax.dynamic_index_in_dim(skip_weight, chan, keepdims=False)
    mixed = conv + skip * x_rows
    tap_count = short_taps.shape[0]
    taps = lax.dynamic_index_in_dim(short_taps, chan, axis=1, keepdims=False)
    even, odd = mixed[:chips], mixed[chips:]
    own_rows = jnp.where(first, even, odd)
    odd_before = jnp.concatenate([jnp.zeros((1, length), mixed.dtype), odd[:-1]], 0)
    earlier = jnp.where(first, odd_before, even)
    joined = jnp.concatenate([own_rows, earlier], 1)
    source = jnp.arange(2 * length, dtype=jnp.int32)
    source = jnp.where(source < length, source, source - 2 * length)
    lag = col_ids[None, :] - source[:, None]
    band = jnp.zeros(lag.shape, mixed.dtype)
    for offset in range(tap_count):
        band = band + jnp.where(lag == offset, taps[offset], 0.0)
    band = lax.optimization_barrier(band)
    back = mat(joined, band)
    short_local = lax.all_to_all(back, "chip", 0, 0, tiled=True)

    groups = lax.axis_size("ch")
    partial = jnp.sum(short_local * short_local, 0)
    spread = jnp.broadcast_to(partial[None], (groups,) + partial.shape)
    energy = jnp.sum(lax.all_to_all(spread, "ch", 0, 0, tiled=True), 0)
    all_channels = width * groups
    return short_local * gains * lax.rsqrt(energy / all_channels + 1e-06)[None, :]


def solution(mesh):
    seq_parts, groups = mesh.devices.shape
    split = jax.sharding.Mesh(mesh.devices.reshape(seq_parts // 2, 2, groups), ("chip", "core", "ch"))
    seq = ("chip", "core")
    return jax.shard_map(
        local,
        mesh=split,
        in_specs=(P("ch", seq), P("ch", seq), P("ch"), P(None, "ch"), P("ch")),
        out_specs=P("ch", seq),
        check_vma=False,
    )
```

```python
import math

import jax
import jax.numpy as jnp
from jax import lax
from jax.sharding import PartitionSpec as P

highest = lax.Precision.HIGH


def phases(left_ids, right_ids, modulus, direction):
    product = left_ids[:, None] * right_ids[None, :] % modulus
    angles = product.astype(jnp.float32) * (2.0 * math.pi / modulus)
    return (jnp.cos(angles), direction * jnp.sin(angles))


def mat(a, b):
    return jnp.dot(a, b, precision=highest, preferred_element_type=jnp.float32)


def cmat(ar, ai, br, bi):
    if ai is None:
        return (mat(ar, br), mat(ar, bi))
    if bi is None:
        return (mat(ar, br), mat(ai, br))
    return (mat(ar, br) - mat(ai, bi), mat(ar, bi) + mat(ai, br))


def cmul(ar, ai, br, bi):
    return (ar * br - ai * bi, ar * bi + ai * br)


def local(signal, long_filter, skip_weight, short_taps, norm_gain):
    seq_parts = lax.axis_size("seq")
    width, length = signal.shape
    dup = seq_parts // width
    piece = length // dup
    own = lax.axis_index("seq")
    chan = own // dup
    half = own % dup
    signal_f = signal.astype(jnp.float32)
    gains = jnp.broadcast_to(norm_gain[:, None], signal.shape)
    gains, signal_f = lax.optimization_barrier((gains, signal_f))

    both = jnp.stack([signal_f, long_filter], 1)
    mine = lax.all_to_all(both.reshape(seq_parts, length), "seq", 0, 0, tiled=True)
    partners = [(i, i ^ 1) for i in range(seq_parts)]
    split = seq_parts // 2
    other_top = lax.ppermute(mine[:split], "seq", partners)
    other_low = lax.ppermute(mine[split:], "seq", partners)
    other = jnp.concatenate([other_top, other_low], 0)
    x_rows = jnp.where(half == 0, mine, other)

    rows = 2 * seq_parts
    cols = length
    modulus = rows * cols
    row_ids = jnp.arange(rows, dtype=jnp.int32)
    col_ids = jnp.arange(cols, dtype=jnp.int32)
    square = phases(col_ids, col_ids, cols, 1.0)
    turn = phases(row_ids, col_ids, modulus, 1.0)
    square, turn = lax.optimization_barrier((square, turn))
    rows_fwd = (square[0][:, :seq_parts], -square[1][:, :seq_parts])
    turn_fwd = (turn[0], -turn[1])
    cols_fwd = (square[0], -square[1])
    cols_inv = square
    rows_inv = (square[0][:seq_parts], square[1][:seq_parts])

    def forward(x):
        yr, yi = cmat(rows_fwd[0], rows_fwd[1], x, None)
        yr, yi = cmul(yr, yi, turn_fwd[0], turn_fwd[1])
        return cmat(yr, yi, cols_fwd[0], cols_fwd[1])

    xr, xi = forward(mine)
    top_r, top_i = cmat(rows_fwd[0][:, :split], rows_fwd[1][:, :split], other_top, None)
    low_r, low_i = cmat(rows_fwd[0][:, split:], rows_fwd[1][:, split:], other_low, None)
    yr, yi = cmul(top_r + low_r, top_i + low_i, turn_fwd[0], turn_fwd[1])
    hr, hi = cmat(yr, yi, cols_fwd[0], cols_fwd[1])
    pr, pi = cmul(xr, xi, hr, hi)
    qr, qi = cmat(pr, pi, cols_inv[0], cols_inv[1])
    qr, qi = cmul(qr, qi, turn_fwd[0], -turn_fwd[1])
    conv = (mat(rows_inv[0], qr) - mat(rows_inv[1], qi)) * (1.0 / modulus)

    skip = lax.dynamic_index_in_dim(skip_weight, chan, keepdims=False)
    mixed = conv + skip * x_rows
    tap_count = short_taps.shape[0]
    taps = lax.dynamic_index_in_dim(short_taps, chan, axis=1, keepdims=False)
    earlier = jnp.concatenate([jnp.zeros((1, length), mixed.dtype), mixed[:-1]], 0)
    joined = jnp.concatenate([mixed, earlier], 1)
    source = jnp.arange(2 * length, dtype=jnp.int32)
    source = jnp.where(source < length, source, source - 2 * length)
    lag = (half * piece + jnp.arange(piece, dtype=jnp.int32))[None, :] - source[:, None]
    band = jnp.zeros(lag.shape, mixed.dtype)
    for offset in range(tap_count):
        band = band + jnp.where(lag == offset, taps[offset], 0.0)
    band = lax.optimization_barrier(band)
    back = mat(joined, band)
    got = lax.all_to_all(back, "seq", 0, 0, tiled=True)
    short_local = got.reshape(width, length)

    groups = lax.axis_size("ch")
    partial = jnp.sum(short_local * short_local, 0)
    spread = jnp.broadcast_to(partial[None], (groups,) + partial.shape)
    energy = jnp.sum(lax.all_to_all(spread, "ch", 0, 0, tiled=True), 0)
    all_channels = width * groups
    return short_local * gains * lax.rsqrt(energy / all_channels + 1e-06)[None, :]


def solution(mesh):
    return jax.shard_map(
        local,
        mesh=mesh,
        in_specs=(P("ch", "seq"), P("ch", "seq"), P("ch"), P(None, "ch"), P("ch")),
        out_specs=P("ch", "seq"),
        check_vma=False,
    )
```
